512 devices in a mesh: dp: 32 (over z, core), expert: 16 (over y, x).
Axes of the slice: x: 4, y: 4, z: 16, core: 2. Of those that a mesh axis runs over, the one named last changes fastest.
Arguments:
- stream: bfloat16 [8192, 2304], P(('dp', 'expert')), may hold values from -6 to 6
- queries: bfloat16 [8192, 2048], P('dp', 'expert'), may hold values from -200 to 200
- key_pages: bfloat16 [1024, 128, 2048], P('dp', None, 'expert'), may hold values from -10.5 to 10.5
- value_pages: bfloat16 [1024, 128, 2048], P('dp', None, 'expert'), may hold values from -6 to 6
- query_counts: int32 [32, 16], P('dp'), may hold values from 1 to 32, 256 in all within a row
- cached_lengths: int32 [32, 16], P('dp'), may hold values from 0 to 224, as said below
- page_tables: int32 [32, 32], P('dp'), may hold values from 0 to 31, each once within a row
- out_proj: bfloat16 [2048, 2304], P('expert'), may hold values from -0.29882812 to 0.29882812
- moe_gain: float32 [2304], replicated, may hold values from 0.1 to 1.9
- router: bfloat16 [2304, 8], replicated, may hold values from -0.125 to 0.125
- gate_proj: bfloat16 [16, 2048, 2304], P('expert', 'dp'), may hold values from -0.125 to 0.125
- up_proj: bfloat16 [16, 2048, 2304], P('expert', 'dp'), may hold values from -0.125 to 0.125
- down_proj: bfloat16 [16, 2048, 2304], P('expert', 'dp'), may hold values from -0.09375 to 0.09375
- routes: int32 [8192, 2], P(('dp', 'expert')), may hold values from 0 to 7, all different within a row; in each aligned block of 16 rows (0 to 15, 16 to 31, ...) at most 6 rows name the same one
- next_gain: float32 [2304], replicated, may hold values from 0.1 to 1.9
Outputs:
- resid_out: bfloat16 [8192, 2304], P(('dp', 'expert'))
- normed_out: bfloat16 [8192, 2304], P(('dp', 'expert'))
The draws below stay inside these ranges and needn't reach their ends.
Inputs may be any that keep to these rules, and one draw needn't show every extreme that they name: `query_counts`: each group's counts sum to 256, and one of them is 32. `cached_lengths`: in each group one sequence has no cached tokens and another has 224. `page_tables`: each group's row is a permutation of its 32 pages; sequence s uses entries s * 2 to s * 2 + 1. `routes`: each row names two different experts; in each device's aligned block of 16 rows no expert is named by more than 6 rows.
All inputs are finite; a program needn't handle non-finite values.
Results may differ from the reference program's by a relative error of at most 0.014.
Values may be sent and summed in bfloat16 or wider, within the bound.
No kernel may reach another device: no remote copies, remote signals or barrier semaphores. Data moves between devices by JAX's collectives and lax.ppermute only.
A program may use at most 64 MiB of HBM per device.

```python
import math
import jax
import jax.numpy as jnp
import numpy as np
from jax import lax

D = 2304
HEADS = 32
FF = 4096
PAGE = 128
SEQS = 16
PAGES_SEQ = 2
QMAX = 32
ROWS_GRP = 256
EXPERTS = 8
ROWS_DEV = 16
CAP = 6
AW = 2048
POOL = 32
BLOCK = 256
TOTAL_ROWS = 8192
TOTAL_PAGES = 1024
BOUND = 3072
N_DP = 32


def draw_cached_lengths(key, part):
    groups = TOTAL_PAGES // POOL
    highest = PAGES_SEQ * PAGE - QMAX
    key_base, key_top, key_low = jax.random.split(jax.random.fold_in(key, 11), 3)
    base = jax.random.randint(key_base, (groups, SEQS), 0, highest + 1)
    top_slot = jax.random.randint(key_top, (groups, 1), 0, SEQS)
    low_slot = (top_slot + 1 + jax.random.randint(key_low, (groups, 1), 0, SEQS - 1)) % SEQS
    columns = jnp.arange(SEQS)[None, :]
    base = jnp.where(columns == top_slot, highest, base)
    base = jnp.where(columns == low_slot, 0, base)
    return base.astype(jnp.int32)


def draw_queries(key, part):
    key_base = jax.random.fold_in(jax.random.fold_in(key, 21), 0)
    shape = (TOTAL_ROWS, AW)
    values = jnp.clip(jax.random.normal(key_base, shape, jnp.float32), -6.0, 6.0)
    return values.astype(jnp.bfloat16)


def draw_key_pages(key, part):
    key_base = jax.random.fold_in(jax.random.fold_in(key, 31), 0)
    shape = (TOTAL_PAGES, PAGE, AW)
    values = jnp.clip(jax.random.normal(key_base, shape, jnp.float32), -6.0, 6.0)
    return values.astype(jnp.bfloat16)


def level_of(stream_key, extent, cuts, least, largest):
    level = 1.0
    for dim, shards_of in cuts:
        draws = jax.random.uniform(jax.random.fold_in(jax.random.fold_in(stream_key, 6), dim), (shards_of,), jnp.float32, least / len(cuts), largest / len(cuts))
        level = level * jnp.repeat(jnp.exp(draws), extent[dim] // shards_of).reshape((-1,) + (1,) * (len(extent) - 1 - dim))
    return level


def length_profile(count, total, bound, lean):
    weights = [(1 << 20) // math.isqrt(rank ** lean) + 1 for rank in range(2, count + 1)]
    spare, holding = total - bound - (count - 1), [1] * (count - 1)
    while spare > 0:
        candidates = [i for i in range(count - 1) if holding[i] < bound]
        mass, left = sum([weights[i] for i in candidates]), spare
        for i in candidates:
            addition = min(bound - holding[i], max(1, left * weights[i] // mass), spare)
            holding[i] = holding[i] + addition
            spare = spare - addition
    return np.array([bound] + holding)


def ragged_sizes(rng, amount, total, limit, skew):
    if amount == 2:
        one = jax.random.randint(rng, (), max(1, total - limit), min(limit, total - 1) + 1)
        return jnp.stack([one, total - one])
    lengths = jnp.asarray(length_profile(amount, total, limit, skew), jnp.int32)
    twos = (amount - 1) // 2
    giver, receiver = lengths[1:1 + 2 * twos:2], lengths[2:2 + 2 * twos:2]
    margin = jnp.minimum(giver - 1, limit - receiver)
    passed = jax.random.randint(jax.random.fold_in(rng, 1), (twos,), 0, 1 << 20) % (margin + 1)
    lengths = lengths.at[1:1 + 2 * twos:2].set(giver - passed).at[2:2 + 2 * twos:2].set(receiver + passed)
    return lengths[jax.random.permutation(jax.random.fold_in(rng, 2), amount)]


def deal_out(rng, own, number, rows, count, top, bound, lean):
    sequence = jax.random.permutation(rng, count)
    heavy_load, common = portions_of(count, rows * top, bound, lean, True), portions_of(count, rows * top, bound, lean, False)
    places = jnp.arange(count)

    def named(lengths, turn):
        used = int((lengths > 0).sum())
        fixed = max(1, used // 4)
        passed = fixed + (places - fixed + turn * (used - fixed)) % max(1, count - fixed)
        return jnp.zeros((count,), jnp.int32).at[sequence[jnp.where(places < fixed, places, passed)]].set(jnp.asarray(lengths, jnp.int32))

    lengths = jnp.where(number % 4 == 0, named(heavy_load, number // 4), named(common, number - number // 4 - 1))
    mixed = jax.random.permutation(jax.random.fold_in(own, 3), count)
    source_of, receiver = mixed[0:count // 2 * 2:2], mixed[1:count // 2 * 2:2]
    margin = jnp.minimum(lengths[source_of] - 1, bound - lengths[receiver]) // 2
    margin = jnp.where((source_of == sequence[0]) | (receiver == sequence[0]) | (lengths[receiver] == 0), 0, jnp.maximum(margin, 0))
    passed = jax.random.randint(jax.random.fold_in(own, 4), (count // 2,), 0, 1 << 20) % (margin + 1)
    lengths = lengths.at[source_of].add(-passed).at[receiver].add(passed)
    labels = jnp.searchsorted(jnp.cumsum(lengths), jnp.arange(rows * top), side="right").astype(jnp.int32)
    listing = labels.reshape(top, rows).T
    listing = listing[jax.random.permutation(jax.random.fold_in(own, 1), rows)]
    turn = jax.random.randint(jax.random.fold_in(own, 2), (rows, 1), 0, top)
    return jnp.take_along_axis(listing, (jnp.arange(top)[None, :] + turn) % top, axis=1)


def portions_of(number_of, total, bound, skew, full):
    weights = [(1 << 20) // math.isqrt(standing ** skew) + 1 for standing in range(1, number_of + 1)]
    largest = bound if full else min(bound, max(-(-total // number_of), total * weights[0] // sum(weights)))
    least = 1 if total - largest >= number_of - 1 else 0
    holding, rest = [largest] + [least] * (number_of - 1), total - largest - least * (number_of - 1)
    while rest > 0:
        free = [i for i in range(1, number_of) if holding[i] < largest] or [i for i in range(1, number_of) if holding[i] < bound]
        pool, budget = sum([weights[i] for i in free]), rest
        for i in free:
            more = min(bound - holding[i], max(1, budget * weights[i] // pool), rest)
            holding[i] = holding[i] + more
            rest = rest - more
    return np.array(holding)


def centred(rng, extent, deviation, bound, pieces=(), held_as=jnp.bfloat16):
    values = deviation * jax.random.normal(rng, extent, jnp.float32)
    if pieces:
        values = values * level_of(rng, extent, pieces, -0.22, 0.18)
    return jnp.clip(values, -bound, bound).astype(held_as)


def setup_inputs(seed: int = 0) -> dict:
    splits = jax.random.split(jax.random.key(seed), 16)
    stream = centred(splits[0], (TOTAL_ROWS, D), 1.0, 6.0, ((0, 512),))
    queries = draw_queries(jax.random.fold_in(splits[15], 71), 0)
    key_pages = draw_key_pages(jax.random.fold_in(splits[15], 71), 0)
    value_pages = centred(splits[3], (TOTAL_PAGES, PAGE, AW), 1.0, 6.0, ((0, 32), (2, 16)))
    query_counts = jax.vmap(lambda own: ragged_sizes(own, SEQS, ROWS_GRP, QMAX, 2))(jax.random.split(splits[4], N_DP)).reshape((N_DP, SEQS)).astype(jnp.int32)
    cached_lengths = draw_cached_lengths(jax.random.fold_in(splits[15], 71), 0)
    page_tables = jax.vmap(lambda own: jax.random.permutation(own, POOL))(jax.random.split(splits[6], N_DP)).reshape((N_DP, POOL)).astype(jnp.int32)
    out_proj = centred(splits[7], (AW, D), 0.05, 0.29882812, ((0, 16),))
    moe_gain = jnp.clip(1.0 + 0.18 * jax.random.normal(splits[8], (D,), jnp.float32), 0.1, 1.9)
    router = centred(splits[9], (D, EXPERTS), D ** -0.5, 0.125)
    gate_proj = centred(splits[10], (2 * EXPERTS, FF // 2, D), D ** -0.5, 0.125, ((0, 16), (1, 32)))
    up_proj = centred(splits[11], (2 * EXPERTS, FF // 2, D), D ** -0.5, 0.125, ((0, 16), (1, 32)))
    down_proj = centred(splits[12], (2 * EXPERTS, FF // 2, D), FF ** -0.5, 0.09375, ((0, 16), (1, 32)))
    routes_keys = jax.random.split(jax.random.fold_in(splits[13], 1), TOTAL_ROWS // ROWS_DEV)
    routes_turns = jax.random.permutation(jax.random.fold_in(splits[13], 3), TOTAL_ROWS // ROWS_DEV)
    routes = jax.vmap(lambda own, number: deal_out(jax.random.fold_in(splits[13], 2), own, number, ROWS_DEV, EXPERTS, 2, CAP, 2))(routes_keys, routes_turns).reshape((TOTAL_ROWS, 2))
    next_gain = jnp.clip(1.0 + 0.18 * jax.random.normal(splits[14], (D,), jnp.float32), 0.1, 1.9)
    return {"stream": stream, "queries": queries, "key_pages": key_pages, "value_pages": value_pages, "query_counts": query_counts, "cached_lengths": cached_lengths, "page_tables": page_tables, "out_proj": out_proj, "moe_gain": moe_gain, "router": router, "gate_proj": gate_proj, "up_proj": up_proj, "down_proj": down_proj, "routes": routes, "next_gain": next_gain}


eps = 1e-06

def rms_scale(values, gain):
    mean_square = lax.optimization_barrier(jnp.mean(values * values, axis=-1, keepdims=True))
    return values * lax.rsqrt(mean_square + eps) * gain

def paged_attention(group_queries, group_keys, group_values, counts, cached, page_table, head_count):
    row_count, lane_count = group_queries.shape
    head_size = lane_count // head_count
    seq_count = counts.shape[0]
    page_count = page_table.shape[0] // seq_count
    page_len = group_keys.shape[1]
    starts = jnp.cumsum(counts) - counts
    slot_ids = jnp.arange(QMAX, dtype=jnp.int32)
    row_index = jnp.clip(starts[:, None] + slot_ids[None, :], 0, row_count - 1).astype(jnp.int32)
    picked = group_queries[row_index].reshape(seq_count, QMAX, head_count, head_size)
    page_ids = page_table.reshape(seq_count, page_count)
    seq_keys = group_keys[page_ids].reshape(seq_count, page_count * page_len, head_count, head_size)
    seq_values = group_values[page_ids].reshape(seq_count, page_count * page_len, head_count, head_size)
    scores = jnp.einsum('sqhd,skhd->shqk', picked.astype(jnp.float32), seq_keys.astype(jnp.float32)) * head_size ** (-0.5)
    key_position = jnp.arange(page_count * page_len, dtype=jnp.int32)
    last_key = cached[:, None] + slot_ids[None, :]
    allowed = key_position[None, None, :] <= last_key[:, :, None]
    scores = jnp.where(allowed[:, None, :, :], scores, -1e+30)
    row_max = lax.optimization_barrier(jnp.max(scores, axis=-1, keepdims=True))
    weights = jnp.exp(scores - row_max)
    row_total = lax.optimization_barrier(jnp.sum(weights, axis=-1, keepdims=True))
    probabilities = weights.astype(jnp.bfloat16)
    attended = jnp.einsum('shqk,skhd->shqd', probabilities.astype(jnp.float32), seq_values.astype(jnp.float32)) / row_total
    attended = attended.astype(jnp.bfloat16).transpose(0, 2, 1, 3).reshape(seq_count, QMAX, lane_count)
    row_ids = jnp.arange(row_count, dtype=jnp.int32)
    owning = (lax.optimization_barrier(jnp.sum((starts[None, :] <= row_ids[:, None]).astype(jnp.int32), axis=1)) - 1).astype(jnp.int32)
    offset = (row_ids - starts[owning]).astype(jnp.int32)
    return attended[owning, offset]

def reference(stream, queries, key_pages, value_pages, query_counts, cached_lengths, page_tables, out_proj, moe_gain, router, gate_proj, up_proj, down_proj, routes, next_gain):
    groups = query_counts.shape[0]

    def one_group(operands):
        group_queries, group_keys, group_values, counts, cached, page_table = operands
        return paged_attention(group_queries, group_keys, group_values, counts, cached, page_table, HEADS)
    attended = lax.map(one_group, (queries.reshape(groups, ROWS_GRP, AW), key_pages.reshape(groups, POOL, PAGE, AW), value_pages.reshape(groups, POOL, PAGE, AW), query_counts, cached_lengths, page_tables)).reshape(TOTAL_ROWS, AW)
    hidden = stream.astype(jnp.float32) + jnp.dot(attended, out_proj, preferred_element_type=jnp.float32)
    normed = rms_scale(hidden, moe_gain).astype(jnp.bfloat16)
    logits = jnp.dot(normed, router, preferred_element_type=jnp.float32)
    chosen = jnp.take_along_axis(logits, routes, axis=1)
    first_share = jax.nn.sigmoid(chosen[:, 0] - chosen[:, 1])
    shares = jnp.stack([first_share, 1.0 - first_share], axis=1)
    gate_full = gate_proj.reshape(EXPERTS, FF, D)
    up_full = up_proj.reshape(EXPERTS, FF, D)
    down_full = down_proj.reshape(EXPERTS, FF, D)
    block_count = FF // BLOCK

    def expert_pass(carry, expert_id):
        gate_rows = lax.dynamic_index_in_dim(gate_full, expert_id, 0, keepdims=False)
        up_rows = lax.dynamic_index_in_dim(up_full, expert_id, 0, keepdims=False)
        down_rows = lax.dynamic_index_in_dim(down_full, expert_id, 0, keepdims=False)
        naming = routes == expert_id
        member = jnp.any(naming, axis=1)
        share = lax.optimization_barrier(jnp.sum(jnp.where(naming, shares, jnp.zeros_like(shares)), axis=1))
        ordering = jnp.argsort(jnp.where(member, 0, 1).astype(jnp.int32), stable=True)[:BOUND].astype(jnp.int32)
        picked = normed[ordering]
        gate_val = jnp.dot(picked, gate_rows.T, preferred_element_type=jnp.float32)
        up_val = jnp.dot(picked, up_rows.T, preferred_element_type=jnp.float32)
        activated = (jax.nn.silu(gate_val) * up_val).astype(jnp.bfloat16)
        act_blocks = activated.reshape(BOUND, block_count, BLOCK).transpose(1, 0, 2)
        down_blocks = down_rows.reshape(block_count, BLOCK, D)

        def add_block(running, operands):
            act_piece, down_piece = operands
            block_part = jnp.dot(act_piece, down_piece, preferred_element_type=jnp.float32).astype(jnp.bfloat16)
            block_part = lax.optimization_barrier(block_part)
            return (running + block_part.astype(jnp.float32), None)
        expert_result, _ = lax.scan(add_block, jnp.zeros((BOUND, D), jnp.float32), (act_blocks, down_blocks))
        picked_share = share[ordering]
        scale_rows = jnp.where(member[ordering], picked_share, jnp.zeros_like(picked_share))
        return (carry.at[ordering].add(expert_result * scale_rows[:, None]), None)
    expert_mix, _ = lax.scan(expert_pass, jnp.zeros((TOTAL_ROWS, D), jnp.float32), jnp.arange(EXPERTS, dtype=jnp.int32))
    combined = hidden + expert_mix
    return (combined.astype(jnp.bfloat16), rms_scale(combined, next_gain).astype(jnp.bfloat16))
```

```python
import jax
import jax.numpy as jnp
from jax import lax
from jax.sharding import PartitionSpec as P

HD = 64
QMAX = 32


eps = 1e-06


def rms_scale(values, gain):
    mean_square = jnp.mean(values * values, axis=-1, keepdims=True)
    return values * lax.rsqrt(mean_square + eps) * gain


def paged_attention(
    group_queries, group_keys, group_values, counts, cached, page_table, head_count
):
    row_count, lane_count = group_queries.shape
    head_size = lane_count // head_count
    seq_count = counts.shape[0]
    page_count = page_table.shape[0] // seq_count
    page_len = group_keys.shape[1]
    starts = jnp.cumsum(counts) - counts
    slot_ids = jnp.arange(QMAX, dtype=jnp.int32)
    row_index = jnp.clip(starts[:, None] + slot_ids[None, :], 0, row_count - 1)
    picked = group_queries[row_index].reshape(seq_count, QMAX, head_count, head_size)
    page_ids = page_table.reshape(seq_count, page_count)
    seq_keys = group_keys[page_ids].reshape(seq_count, page_count * page_len, head_count, head_size)
    seq_values = group_values[page_ids].reshape(
        seq_count, page_count * page_len, head_count, head_size
    )
    scores = jnp.einsum(
        "sqhd,skhd->shqk", picked, seq_keys, preferred_element_type=jnp.float32
    ) * head_size ** (-0.5)
    key_position = jnp.arange(page_count * page_len, dtype=jnp.int32)
    last_key = cached[:, None] + slot_ids[None, :]
    allowed = key_position[None, None, :] <= last_key[:, :, None]
    scores = jnp.where(allowed[:, None, :, :], scores, -1e30)
    row_max = jnp.max(scores, axis=-1, keepdims=True)
    weights = jnp.exp(scores - row_max)
    row_total = jnp.sum(weights, axis=-1, keepdims=True)
    probabilities = weights.astype(jnp.bfloat16)
    attended = (
        jnp.einsum("shqk,skhd->shqd", probabilities, seq_values, preferred_element_type=jnp.float32)
        / row_total
    )
    attended = (
        attended.astype(jnp.bfloat16).transpose(0, 2, 1, 3).reshape(seq_count, QMAX, lane_count)
    )
    row_ids = jnp.arange(row_count, dtype=jnp.int32)
    owning = jnp.sum((starts[None, :] <= row_ids[:, None]).astype(jnp.int32), axis=1) - 1
    offset = row_ids - starts[owning]
    return attended[owning, offset]


def on_device(
    stream,
    queries,
    key_pages,
    value_pages,
    query_counts,
    cached_lengths,
    page_tables,
    out_proj,
    moe_gain,
    router,
    gate_proj,
    up_proj,
    down_proj,
    routes,
    next_gain,
):
    held = lax.all_gather(
        jnp.stack([gate_proj[0], up_proj[0], down_proj[0]]), "zz", axis=1, tiled=True
    )
    gate_held = held[0]
    up_held = held[1]
    down_held = held[2]
    heads_here = queries.shape[1] // HD
    attended = paged_attention(
        queries,
        key_pages,
        value_pages,
        query_counts[0],
        cached_lengths[0],
        page_tables[0],
        heads_here,
    )
    own_rows = stream.shape[0]
    partial_proj = jnp.dot(attended, out_proj, preferred_element_type=jnp.float32).astype(
        jnp.bfloat16
    )
    expert_count = lax.axis_size("expert")
    gathered_proj = lax.all_to_all(
        partial_proj.reshape(expert_count, own_rows, partial_proj.shape[1]),
        "expert",
        split_axis=0,
        concat_axis=0,
        tiled=True,
    )
    projected = jnp.sum(gathered_proj.astype(jnp.float32), axis=0)
    hidden = stream.astype(jnp.float32) + projected
    normed = rms_scale(hidden, moe_gain).astype(jnp.bfloat16)
    logits = jnp.dot(normed, router, preferred_element_type=jnp.float32)
    chosen = jnp.take_along_axis(logits, routes, axis=1)
    first_share = jax.nn.sigmoid(chosen[:, 0] - chosen[:, 1])
    shares = jnp.stack([first_share, 1.0 - first_share], axis=1)
    expert_devs = lax.axis_size("expert")
    experts_all = expert_devs // 2
    model_width = stream.shape[1]
    capacity = max(2, min(own_rows, 3 * own_rows // experts_all))
    flat_routes = routes.reshape(-1)
    onehot = (flat_routes[:, None] == jnp.arange(experts_all, dtype=jnp.int32)[None, :]).astype(
        jnp.int32
    )
    earlier = jnp.cumsum(onehot, axis=0) - onehot
    position = jnp.sum(earlier * onehot, axis=1)
    target = flat_routes * capacity + position
    placing = (
        jnp.arange(experts_all * capacity, dtype=jnp.int32)[:, None] == target[None, :]
    ).astype(jnp.bfloat16)
    repeated = jnp.repeat(normed, 2, axis=0)
    packed = jnp.dot(placing, repeated, preferred_element_type=jnp.float32).astype(jnp.bfloat16)
    packed = packed.reshape(experts_all, 1, capacity, model_width)
    outgoing = jnp.broadcast_to(packed, (experts_all, 2, capacity, model_width))
    arrived = lax.all_to_all(
        outgoing.reshape(expert_devs * capacity, model_width),
        "expert",
        split_axis=0,
        concat_axis=0,
        tiled=True,
    )
    n_zz = lax.axis_size("zz")
    n_h = lax.axis_size("h")
    n_c = lax.axis_size("c")
    slot_total = arrived.shape[0]
    piece = slot_total // n_zz
    sent = lax.all_to_all(
        arrived.reshape(n_zz, piece, model_width), "zz", split_axis=0, concat_axis=0, tiled=True
    )
    over_h = lax.all_gather(sent, "h")
    rows_here = lax.all_gather(over_h, "c")
    flat_rows = rows_here.reshape(n_c * n_h * n_zz * piece, model_width)
    gate_val = lax.dot_general(
        flat_rows, gate_held, (((1,), (1,)), ((), ())), preferred_element_type=jnp.float32
    )
    up_val = lax.dot_general(
        flat_rows, up_held, (((1,), (1,)), ((), ())), preferred_element_type=jnp.float32
    )
    activated = (jax.nn.silu(gate_val) * up_val).astype(jnp.bfloat16)
    partial = jnp.dot(activated, down_held, preferred_element_type=jnp.float32).astype(jnp.bfloat16)
    partial = partial.reshape(n_c, n_h, n_zz, piece, model_width)
    back_c = lax.all_to_all(partial, "c", split_axis=0, concat_axis=0, tiled=True)
    back_h = lax.all_to_all(back_c, "h", split_axis=1, concat_axis=1, tiled=True)
    summed = jnp.sum(back_h.astype(jnp.float32), axis=(0, 1)).astype(jnp.bfloat16)
    own_slots = lax.all_to_all(summed, "zz", split_axis=0, concat_axis=0, tiled=True)
    returned = lax.all_to_all(
        own_slots.reshape(slot_total, model_width), "expert", split_axis=0, concat_axis=0, tiled=True
    ).astype(jnp.float32)
    arranged = returned.reshape(experts_all, 2, capacity, model_width)
    expert_result = jnp.sum(arranged, axis=1)
    per_slot = expert_result.reshape(experts_all * capacity, model_width)[target]
    expert_mix = jnp.sum(per_slot.reshape(own_rows, 2, model_width) * shares[:, :, None], axis=1)
    combined = hidden + expert_mix
    return (combined.astype(jnp.bfloat16), rms_scale(combined, next_gain).astype(jnp.bfloat16))


def solution(mesh):
    n_dp = mesh.shape["dp"]
    n_chips = n_dp // 2
    split = jax.sharding.Mesh(
        mesh.devices.reshape(n_chips // 4, 4, 2, mesh.shape["expert"]), ("zz", "h", "c", "expert")
    )
    dp = ("zz", "h", "c")
    placed = (
        P((*dp, "expert"), None),
        P(dp, "expert"),
        P(dp, None, "expert"),
        P(dp, None, "expert"),
        P(dp, None),
        P(dp, None),
        P(dp, None),
        P("expert", None),
        P(),
        P(),
        P("expert", dp, None),
        P("expert", dp, None),
        P("expert", dp, None),
        P((*dp, "expert"), None),
        P(),
    )

    return jax.shard_map(
        on_device,
        mesh=split,
        in_specs=placed,
        out_specs=(P((*dp, "expert"), None), P((*dp, "expert"), None)),
        check_vma=False,
    )
```

```python
import jax
import jax.numpy as jnp
from jax import lax
from jax.sharding import PartitionSpec as P

HD = 64
QMAX = 32


eps = 1e-06


def rms_scale(values, gain):
    mean_square = jnp.mean(values * values, axis=-1, keepdims=True)
    return values * lax.rsqrt(mean_square + eps) * gain


def paged_attention(
    group_queries, group_keys, group_values, counts, cached, page_table, head_count
):
    row_count, lane_count = group_queries.shape
    head_size = lane_count // head_count
    seq_count = counts.shape[0]
    page_count = page_table.shape[0] // seq_count
    page_len = group_keys.shape[1]
    starts = jnp.cumsum(counts) - counts
    slot_ids = jnp.arange(QMAX, dtype=jnp.int32)
    row_index = jnp.clip(starts[:, None] + slot_ids[None, :], 0, row_count - 1)
    picked = group_queries[row_index].reshape(seq_count, QMAX, head_count, head_size)
    page_ids = page_table.reshape(seq_count, page_count)
    seq_keys = group_keys[page_ids].reshape(seq_count, page_count * page_len, head_count, head_size)
    seq_values = group_values[page_ids].reshape(
        seq_count, page_count * page_len, head_count, head_size
    )
    scores = jnp.einsum(
        "sqhd,skhd->shqk", picked, seq_keys, preferred_element_type=jnp.float32
    ) * head_size ** (-0.5)
    key_position = jnp.arange(page_count * page_len, dtype=jnp.int32)
    last_key = cached[:, None] + slot_ids[None, :]
    allowed = key_position[None, None, :] <= last_key[:, :, None]
    scores = jnp.where(allowed[:, None, :, :], scores, -1e30)
    row_max = jnp.max(scores, axis=-1, keepdims=True)
    weights = jnp.exp(scores - row_max)
    row_total = jnp.sum(weights, axis=-1, keepdims=True)
    probabilities = weights.astype(jnp.bfloat16)
    attended = (
        jnp.einsum("shqk,skhd->shqd", probabilities, seq_values, preferred_element_type=jnp.float32)
        / row_total
    )
    attended = (
        attended.astype(jnp.bfloat16).transpose(0, 2, 1, 3).reshape(seq_count, QMAX, lane_count)
    )
    row_ids = jnp.arange(row_count, dtype=jnp.int32)
    owning = jnp.sum((starts[None, :] <= row_ids[:, None]).astype(jnp.int32), axis=1) - 1
    offset = row_ids - starts[owning]
    return attended[owning, offset]


def on_device(
    stream,
    queries,
    key_pages,
    value_pages,
    query_counts,
    cached_lengths,
    page_tables,
    out_proj,
    moe_gain,
    router,
    gate_proj,
    up_proj,
    down_proj,
    routes,
    next_gain,
):
    held = lax.all_gather(
        jnp.stack([gate_proj[0], up_proj[0], down_proj[0]]), "zz", axis=1, tiled=True
    )
    gate_held = held[0]
    up_held = held[1]
    down_held = held[2]
    heads_here = queries.shape[1] // HD
    attended = paged_attention(
        queries,
        key_pages,
        value_pages,
        query_counts[0],
        cached_lengths[0],
        page_tables[0],
        heads_here,
    )
    own_rows = stream.shape[0]
    partial_proj = jnp.dot(attended, out_proj, preferred_element_type=jnp.float32).astype(
        jnp.bfloat16
    )
    expert_count = lax.axis_size("expert")
    gathered_proj = lax.all_to_all(
        partial_proj.reshape(expert_count, own_rows, partial_proj.shape[1]),
        "expert",
        split_axis=0,
        concat_axis=0,
        tiled=True,
    )
    projected = jnp.sum(gathered_proj.astype(jnp.float32), axis=0)
    hidden = stream.astype(jnp.float32) + projected
    normed = rms_scale(hidden, moe_gain).astype(jnp.bfloat16)
    logits = jnp.dot(normed, router, preferred_element_type=jnp.float32)
    chosen = jnp.take_along_axis(logits, routes, axis=1)
    first_share = jax.nn.sigmoid(chosen[:, 0] - chosen[:, 1])
    shares = jnp.stack([first_share, 1.0 - first_share], axis=1)
    expert_devs = lax.axis_size("expert")
    experts_all = expert_devs // 2
    model_width = stream.shape[1]
    capacity = max(2, min(own_rows, 3 * own_rows // experts_all))
    flat_routes = routes.reshape(-1)
    onehot = (flat_routes[:, None] == jnp.arange(experts_all, dtype=jnp.int32)[None, :]).astype(
        jnp.int32
    )
    earlier = jnp.cumsum(onehot, axis=0) - onehot
    position = jnp.sum(earlier * onehot, axis=1)
    target = flat_routes * capacity + position
    placing = (
        jnp.arange(experts_all * capacity, dtype=jnp.int32)[:, None] == target[None, :]
    ).astype(jnp.bfloat16)
    repeated = jnp.repeat(normed, 2, axis=0)
    packed = jnp.dot(placing, repeated, preferred_element_type=jnp.float32).astype(jnp.bfloat16)
    packed = packed.reshape(experts_all, 1, capacity, model_width)
    outgoing = jnp.broadcast_to(packed, (experts_all, 2, capacity, model_width))
    arrived = lax.all_to_all(
        outgoing.reshape(expert_devs * capacity, model_width),
        "expert",
        split_axis=0,
        concat_axis=0,
        tiled=True,
    )
    n_zz = lax.axis_size("zz")
    n_h = lax.axis_size("h")
    n_c = lax.axis_size("c")
    slot_total = arrived.shape[0]
    piece = slot_total // n_zz
    sent = lax.all_to_all(
        arrived.reshape(n_zz, piece, model_width), "zz", split_axis=0, concat_axis=0, tiled=True
    )
    swap = [(0, 1), (1, 0)]
    from_h = lax.ppermute(sent, "h", swap)
    both_h = jnp.stack([sent, from_h])
    from_c = lax.ppermute(both_h, "c", swap)
    rows_here = jnp.stack([both_h, from_c])
    flat_rows = rows_here.reshape(n_c * n_h * n_zz * piece, model_width)
    gate_val = lax.dot_general(
        flat_rows, gate_held, (((1,), (1,)), ((), ())), preferred_element_type=jnp.float32
    )
    up_val = lax.dot_general(
        flat_rows, up_held, (((1,), (1,)), ((), ())), preferred_element_type=jnp.float32
    )
    activated = (jax.nn.silu(gate_val) * up_val).astype(jnp.bfloat16)
    partial = jnp.dot(activated, down_held, preferred_element_type=jnp.float32).astype(jnp.bfloat16)
    partial = partial.reshape(n_c, n_h, n_zz, piece, model_width)
    back_c = lax.ppermute(partial[1], "c", swap)
    sum_c = (partial[0].astype(jnp.float32) + back_c.astype(jnp.float32)).astype(jnp.bfloat16)
    back_h = lax.ppermute(sum_c[1], "h", swap)
    summed = (sum_c[0].astype(jnp.float32) + back_h.astype(jnp.float32)).astype(jnp.bfloat16)
    own_slots = lax.all_to_all(summed, "zz", split_axis=0, concat_axis=0, tiled=True)
    returned = lax.all_to_all(
        own_slots.reshape(slot_total, model_width), "expert", split_axis=0, concat_axis=0, tiled=True
    ).astype(jnp.float32)
    arranged = returned.reshape(experts_all, 2, capacity, model_width)
    expert_result = jnp.sum(arranged, axis=1)
    per_slot = expert_result.reshape(experts_all * capacity, model_width)[target]
    expert_mix = jnp.sum(per_slot.reshape(own_rows, 2, model_width) * shares[:, :, None], axis=1)
    combined = hidden + expert_mix
    return (combined.astype(jnp.bfloat16), rms_scale(combined, next_gain).astype(jnp.bfloat16))


def solution(mesh):
    n_dp = mesh.shape["dp"]
    n_chips = n_dp // 2
    split = jax.sharding.Mesh(
        mesh.devices.reshape(n_chips // 2, 2, 2, mesh.shape["expert"]), ("zz", "h", "c", "expert")
    )
    dp = ("zz", "h", "c")
    placed = (
        P((*dp, "expert"), None),
        P(dp, "expert"),
        P(dp, None, "expert"),
        P(dp, None, "expert"),
        P(dp, None),
        P(dp, None),
        P(dp, None),
        P("expert", None),
        P(),
        P(),
        P("expert", dp, None),
        P("expert", dp, None),
        P("expert", dp, None),
        P((*dp, "expert"), None),
        P(),
    )

    return jax.shard_map(
        on_device,
        mesh=split,
        in_specs=placed,
        out_specs=(P((*dp, "expert"), None), P((*dp, "expert"), None)),
        check_vma=False,
    )
```

```python
import jax
import jax.numpy as jnp
from jax import lax
from jax.sharding import PartitionSpec as P

HD = 64
QMAX = 32


eps = 1e-06


def rms_scale(values, gain):
    mean_square = jnp.mean(values * values, axis=-1, keepdims=True)
    return values * lax.rsqrt(mean_square + eps) * gain


def paged_attention(
    group_queries, group_keys, group_values, counts, cached, page_table, head_count
):
    row_count, lane_count = group_queries.shape
    head_size = lane_count // head_count
    seq_count = counts.shape[0]
    page_count = page_table.shape[0] // seq_count
    page_len = group_keys.shape[1]
    starts = jnp.cumsum(counts) - counts
    slot_ids = jnp.arange(QMAX, dtype=jnp.int32)
    row_index = jnp.clip(starts[:, None] + slot_ids[None, :], 0, row_count - 1)
    picked = group_queries[row_index].reshape(seq_count, QMAX, head_count, head_size)
    page_ids = page_table.reshape(seq_count, page_count)
    seq_keys = group_keys[page_ids].reshape(seq_count, page_count * page_len, head_count, head_size)
    seq_values = group_values[page_ids].reshape(
        seq_count, page_count * page_len, head_count, head_size
    )
    scores = jnp.einsum(
        "sqhd,skhd->shqk", picked, seq_keys, preferred_element_type=jnp.float32
    ) * head_size ** (-0.5)
    key_position = jnp.arange(page_count * page_len, dtype=jnp.int32)
    last_key = cached[:, None] + slot_ids[None, :]
    allowed = key_position[None, None, :] <= last_key[:, :, None]
    scores = jnp.where(allowed[:, None, :, :], scores, -1e30)
    row_max = jnp.max(scores, axis=-1, keepdims=True)
    weights = jnp.exp(scores - row_max)
    row_total = jnp.sum(weights, axis=-1, keepdims=True)
    probabilities = weights.astype(jnp.bfloat16)
    attended = (
        jnp.einsum("shqk,skhd->shqd", probabilities, seq_values, preferred_element_type=jnp.float32)
        / row_total
    )
    attended = (
        attended.astype(jnp.bfloat16).transpose(0, 2, 1, 3).reshape(seq_count, QMAX, lane_count)
    )
    row_ids = jnp.arange(row_count, dtype=jnp.int32)
    owning = jnp.sum((starts[None, :] <= row_ids[:, None]).astype(jnp.int32), axis=1) - 1
    offset = row_ids - starts[owning]
    return attended[owning, offset]


def on_device(
    stream,
    queries,
    key_pages,
    value_pages,
    query_counts,
    cached_lengths,
    page_tables,
    out_proj,
    moe_gain,
    router,
    gate_proj,
    up_proj,
    down_proj,
    routes,
    next_gain,
):
    held = lax.all_gather(
        jnp.stack([gate_proj[0], up_proj[0], down_proj[0]]), "zz", axis=1, tiled=True
    )
    gate_held = held[0]
    up_held = held[1]
    down_held = held[2]
    heads_here = queries.shape[1] // HD
    attended = paged_attention(
        queries,
        key_pages,
        value_pages,
        query_counts[0],
        cached_lengths[0],
        page_tables[0],
        heads_here,
    )
    own_rows = stream.shape[0]
    partial_proj = jnp.dot(attended, out_proj, preferred_element_type=jnp.float32).astype(
        jnp.bfloat16
    )
    expert_count = lax.axis_size("expert")
    gathered_proj = lax.all_to_all(
        partial_proj.reshape(expert_count, own_rows, partial_proj.shape[1]),
        "expert",
        split_axis=0,
        concat_axis=0,
        tiled=True,
    )
    projected = jnp.sum(gathered_proj.astype(jnp.float32), axis=0)
    hidden = stream.astype(jnp.float32) + projected
    normed = rms_scale(hidden, moe_gain).astype(jnp.bfloat16)
    logits = jnp.dot(normed, router, preferred_element_type=jnp.float32)
    chosen = jnp.take_along_axis(logits, routes, axis=1)
    first_share = jax.nn.sigmoid(chosen[:, 0] - chosen[:, 1])
    shares = jnp.stack([first_share, 1.0 - first_share], axis=1)
    expert_devs = lax.axis_size("expert")
    experts_all = expert_devs // 2
    model_width = stream.shape[1]
    capacity = max(2, min(own_rows, 3 * own_rows // experts_all))
    flat_routes = routes.reshape(-1)
    onehot = (flat_routes[:, None] == jnp.arange(experts_all, dtype=jnp.int32)[None, :]).astype(
        jnp.int32
    )
    earlier = jnp.cumsum(onehot, axis=0) - onehot
    position = jnp.sum(earlier * onehot, axis=1)
    target = flat_routes * capacity + position
    placing = (
        jnp.arange(experts_all * capacity, dtype=jnp.int32)[:, None] == target[None, :]
    ).astype(jnp.bfloat16)
    repeated = jnp.repeat(normed, 2, axis=0)
    packed = jnp.dot(placing, repeated, preferred_element_type=jnp.float32).astype(jnp.bfloat16)
    packed = packed.reshape(experts_all, 1, capacity, model_width)
    outgoing = jnp.broadcast_to(packed, (experts_all, 2, capacity, model_width))
    arrived = lax.all_to_all(
        outgoing.reshape(expert_devs * capacity, model_width),
        "expert",
        split_axis=0,
        concat_axis=0,
        tiled=True,
    )
    n_zz = lax.axis_size("zz")
    n_h = lax.axis_size("h")
    n_c = lax.axis_size("c")
    slot_total = arrived.shape[0]
    piece = slot_total // n_zz
    zz_index = lax.axis_index("zz")
    by_piece = arrived.reshape(n_zz, piece, model_width)
    rolled = lax.dynamic_slice_in_dim(jnp.concatenate([by_piece, by_piece]), zz_index, n_zz, axis=0)
    sent = jnp.stack(
        [rolled[0]]
        + [
            lax.ppermute(rolled[k], "zz", [(i, (i + k) % n_zz) for i in range(n_zz)])
            for k in range(1, n_zz)
        ]
    )
    swap = [(0, 1), (1, 0)]
    from_h = lax.ppermute(sent, "h", swap)
    both_h = jnp.stack([sent, from_h])
    from_c = lax.ppermute(both_h, "c", swap)
    rows_here = jnp.stack([both_h, from_c])
    flat_rows = rows_here.reshape(n_c * n_h * n_zz * piece, model_width)
    gate_val = lax.dot_general(
        flat_rows, gate_held, (((1,), (1,)), ((), ())), preferred_element_type=jnp.float32
    )
    up_val = lax.dot_general(
        flat_rows, up_held, (((1,), (1,)), ((), ())), preferred_element_type=jnp.float32
    )
    activated = (jax.nn.silu(gate_val) * up_val).astype(jnp.bfloat16)
    partial = jnp.dot(activated, down_held, preferred_element_type=jnp.float32).astype(jnp.bfloat16)
    partial = partial.reshape(n_c, n_h, n_zz, piece, model_width)
    back_c = lax.ppermute(partial[1], "c", swap)
    sum_c = (partial[0].astype(jnp.float32) + back_c.astype(jnp.float32)).astype(jnp.bfloat16)
    back_h = lax.ppermute(sum_c[1], "h", swap)
    summed = (sum_c[0].astype(jnp.float32) + back_h.astype(jnp.float32)).astype(jnp.bfloat16)
    back_rel = jnp.stack(
        [summed[0]]
        + [
            lax.ppermute(summed[k], "zz", [(i, (i - k) % n_zz) for i in range(n_zz)])
            for k in range(1, n_zz)
        ]
    )
    own_slots = lax.dynamic_slice_in_dim(
        jnp.concatenate([back_rel, back_rel]), (n_zz - zz_index) % n_zz, n_zz, axis=0
    )
    returned = lax.all_to_all(
        own_slots.reshape(slot_total, model_width), "expert", split_axis=0, concat_axis=0, tiled=True
    ).astype(jnp.float32)
    arranged = returned.reshape(experts_all, 2, capacity, model_width)
    expert_result = jnp.sum(arranged, axis=1)
    per_slot = expert_result.reshape(experts_all * capacity, model_width)[target]
    expert_mix = jnp.sum(per_slot.reshape(own_rows, 2, model_width) * shares[:, :, None], axis=1)
    combined = hidden + expert_mix
    return (combined.astype(jnp.bfloat16), rms_scale(combined, next_gain).astype(jnp.bfloat16))


def solution(mesh):
    n_dp = mesh.shape["dp"]
    n_chips = n_dp // 2
    split = jax.sharding.Mesh(
        mesh.devices.reshape(n_chips // 2, 2, 2, mesh.shape["expert"]), ("zz", "h", "c", "expert")
    )
    dp = ("zz", "h", "c")
    placed = (
        P((*dp, "expert"), None),
        P(dp, "expert"),
        P(dp, None, "expert"),
        P(dp, None, "expert"),
        P(dp, None),
        P(dp, None),
        P(dp, None),
        P("expert", None),
        P(),
        P(),
        P("expert", dp, None),
        P("expert", dp, None),
        P("expert", dp, None),
        P((*dp, "expert"), None),
        P(),
    )

    return jax.shard_map(
        on_device,
        mesh=split,
        in_specs=placed,
        out_specs=(P((*dp, "expert"), None), P((*dp, "expert"), None)),
        check_vma=False,
    )
```

```python
import jax
import jax.numpy as jnp
from jax import lax
from jax.sharding import PartitionSpec as P

HD = 64
QMAX = 32


eps = 1e-06


def rms_scale(values, gain):
    mean_square = jnp.mean(values * values, axis=-1, keepdims=True)
    return values * lax.rsqrt(mean_square + eps) * gain


def paged_attention(
    group_queries, group_keys, group_values, counts, cached, page_table, head_count
):
    row_count, lane_count = group_queries.shape
    head_size = lane_count // head_count
    seq_count = counts.shape[0]
    page_count = page_table.shape[0] // seq_count
    page_len = group_keys.shape[1]
    starts = jnp.cumsum(counts) - counts
    slot_ids = jnp.arange(QMAX, dtype=jnp.int32)
    row_index = jnp.clip(starts[:, None] + slot_ids[None, :], 0, row_count - 1)
    picked = group_queries[row_index].reshape(seq_count, QMAX, head_count, head_size)
    page_ids = page_table.reshape(seq_count, page_count)
    seq_keys = group_keys[page_ids].reshape(seq_count, page_count * page_len, head_count, head_size)
    seq_values = group_values[page_ids].reshape(
        seq_count, page_count * page_len, head_count, head_size
    )
    scores = jnp.einsum(
        "sqhd,skhd->shqk", picked, seq_keys, preferred_element_type=jnp.float32
    ) * head_size ** (-0.5)
    key_position = jnp.arange(page_count * page_len, dtype=jnp.int32)
    last_key = cached[:, None] + slot_ids[None, :]
    allowed = key_position[None, None, :] <= last_key[:, :, None]
    scores = jnp.where(allowed[:, None, :, :], scores, -1e30)
    row_max = jnp.max(scores, axis=-1, keepdims=True)
    weights = jnp.exp(scores - row_max)
    row_total = jnp.sum(weights, axis=-1, keepdims=True)
    probabilities = weights.astype(jnp.bfloat16)
    attended = (
        jnp.einsum("shqk,skhd->shqd", probabilities, seq_values, preferred_element_type=jnp.float32)
        / row_total
    )
    attended = (
        attended.astype(jnp.bfloat16).transpose(0, 2, 1, 3).reshape(seq_count, QMAX, lane_count)
    )
    row_ids = jnp.arange(row_count, dtype=jnp.int32)
    owning = jnp.sum((starts[None, :] <= row_ids[:, None]).astype(jnp.int32), axis=1) - 1
    offset = row_ids - starts[owning]
    return attended[owning, offset]


def on_device(
    stream,
    queries,
    key_pages,
    value_pages,
    query_counts,
    cached_lengths,
    page_tables,
    out_proj,
    moe_gain,
    router,
    gate_proj,
    up_proj,
    down_proj,
    routes,
    next_gain,
):
    held = lax.all_gather(jnp.stack([gate_proj[0], up_proj[0]]), "zz", axis=1, tiled=True)
    down_held = lax.all_gather(down_proj[0], "zz", axis=0, tiled=True)
    gate_held = held[0]
    up_held = held[1]
    heads_here = queries.shape[1] // HD
    attended = paged_attention(
        queries,
        key_pages,
        value_pages,
        query_counts[0],
        cached_lengths[0],
        page_tables[0],
        heads_here,
    )
    own_rows = stream.shape[0]
    partial_proj = jnp.dot(attended, out_proj, preferred_element_type=jnp.float32).astype(
        jnp.bfloat16
    )
    expert_count = lax.axis_size("expert")
    gathered_proj = lax.all_to_all(
        partial_proj.reshape(expert_count, own_rows, partial_proj.shape[1]),
        "expert",
        split_axis=0,
        concat_axis=0,
        tiled=True,
    )
    projected = jnp.sum(gathered_proj.astype(jnp.float32), axis=0)
    hidden = stream.astype(jnp.float32) + projected
    normed = rms_scale(hidden, moe_gain).astype(jnp.bfloat16)
    logits = jnp.dot(normed, router, preferred_element_type=jnp.float32)
    chosen = jnp.take_along_axis(logits, routes, axis=1)
    first_share = jax.nn.sigmoid(chosen[:, 0] - chosen[:, 1])
    shares = jnp.stack([first_share, 1.0 - first_share], axis=1)
    expert_devs = lax.axis_size("expert")
    experts_all = expert_devs // 2
    model_width = stream.shape[1]
    capacity = max(2, min(own_rows, 3 * own_rows // experts_all))
    flat_routes = routes.reshape(-1)
    onehot = (flat_routes[:, None] == jnp.arange(experts_all, dtype=jnp.int32)[None, :]).astype(
        jnp.int32
    )
    earlier = jnp.cumsum(onehot, axis=0) - onehot
    position = jnp.sum(earlier * onehot, axis=1)
    target = flat_routes * capacity + position
    placing = (
        jnp.arange(experts_all * capacity, dtype=jnp.int32)[:, None] == target[None, :]
    ).astype(jnp.bfloat16)
    repeated = jnp.repeat(normed, 2, axis=0)
    packed = jnp.dot(placing, repeated, preferred_element_type=jnp.float32).astype(jnp.bfloat16)
    packed = packed.reshape(experts_all, 1, capacity, model_width)
    outgoing = jnp.broadcast_to(packed, (experts_all, 2, capacity, model_width))
    arrived = lax.all_to_all(
        outgoing.reshape(expert_devs * capacity, model_width),
        "expert",
        split_axis=0,
        concat_axis=0,
        tiled=True,
    )
    n_zz = lax.axis_size("zz")
    n_h = lax.axis_size("h")
    n_c = lax.axis_size("c")
    slot_total = arrived.shape[0]
    piece = slot_total // n_zz
    sent = lax.all_to_all(
        arrived.reshape(n_zz, piece, model_width), "zz", split_axis=0, concat_axis=0, tiled=True
    )
    swap = [(0, 1), (1, 0)]
    from_h = lax.ppermute(sent, "h", swap)
    both_h = jnp.stack([sent, from_h])
    from_c = lax.ppermute(both_h, "c", swap)
    rows_here = jnp.stack([both_h, from_c])
    flat_rows = rows_here.reshape(n_c * n_h * n_zz * piece, model_width)
    gate_val = lax.dot_general(
        flat_rows, gate_held, (((1,), (1,)), ((), ())), preferred_element_type=jnp.float32
    )
    up_val = lax.dot_general(
        flat_rows, up_held, (((1,), (1,)), ((), ())), preferred_element_type=jnp.float32
    )
    activated = (jax.nn.silu(gate_val) * up_val).astype(jnp.bfloat16)
    partial = jnp.dot(activated, down_held, preferred_element_type=jnp.float32).astype(jnp.bfloat16)
    partial = partial.reshape(n_c, n_h, n_zz, piece, model_width)
    back_c = lax.ppermute(partial[1], "c", swap)
    sum_c = (partial[0].astype(jnp.float32) + back_c.astype(jnp.float32)).astype(jnp.bfloat16)
    back_h = lax.ppermute(sum_c[1], "h", swap)
    summed = (sum_c[0].astype(jnp.float32) + back_h.astype(jnp.float32)).astype(jnp.bfloat16)
    own_slots = lax.all_to_all(summed, "zz", split_axis=0, concat_axis=0, tiled=True)
    returned = lax.all_to_all(
        own_slots.reshape(slot_total, model_width), "expert", split_axis=0, concat_axis=0, tiled=True
    ).astype(jnp.float32)
    arranged = returned.reshape(experts_all, 2, capacity, model_width)
    expert_result = jnp.sum(arranged, axis=1)
    per_slot = expert_result.reshape(experts_all * capacity, model_width)[target]
    expert_mix = jnp.sum(per_slot.reshape(own_rows, 2, model_width) * shares[:, :, None], axis=1)
    combined = hidden + expert_mix
    return (combined.astype(jnp.bfloat16), rms_scale(combined, next_gain).astype(jnp.bfloat16))


def solution(mesh):
    n_dp = mesh.shape["dp"]
    n_chips = n_dp // 2
    split = jax.sharding.Mesh(
        mesh.devices.reshape(n_chips // 2, 2, 2, mesh.shape["expert"]), ("zz", "h", "c", "expert")
    )
    dp = ("zz", "h", "c")
    placed = (
        P((*dp, "expert"), None),
        P(dp, "expert"),
        P(dp, None, "expert"),
        P(dp, None, "expert"),
        P(dp, None),
        P(dp, None),
        P(dp, None),
        P("expert", None),
        P(),
        P(),
        P("expert", dp, None),
        P("expert", dp, None),
        P("expert", dp, None),
        P((*dp, "expert"), None),
        P(),
    )

    return jax.shard_map(
        on_device,
        mesh=split,
        in_specs=placed,
        out_specs=(P((*dp, "expert"), None), P((*dp, "expert"), None)),
        check_vma=False,
    )
```

```python
import jax
import jax.numpy as jnp
from jax import lax
from jax.sharding import PartitionSpec as P

HD = 64
QMAX = 32


eps = 1e-06


def rms_scale(values, gain):
    mean_square = jnp.mean(values * values, axis=-1, keepdims=True)
    return values * lax.rsqrt(mean_square + eps) * gain


def paged_attention(
    group_queries, group_keys, group_values, counts, cached, page_table, head_count
):
    row_count, lane_count = group_queries.shape
    head_size = lane_count // head_count
    seq_count = counts.shape[0]
    page_count = page_table.shape[0] // seq_count
    page_len = group_keys.shape[1]
    starts = jnp.cumsum(counts) - counts
    slot_ids = jnp.arange(QMAX, dtype=jnp.int32)
    row_index = jnp.clip(starts[:, None] + slot_ids[None, :], 0, row_count - 1)
    picked = group_queries[row_index].reshape(seq_count, QMAX, head_count, head_size)
    page_ids = page_table.reshape(seq_count, page_count)
    seq_keys = group_keys[page_ids].reshape(seq_count, page_count * page_len, head_count, head_size)
    seq_values = group_values[page_ids].reshape(
        seq_count, page_count * page_len, head_count, head_size
    )
    scores = jnp.einsum(
        "sqhd,skhd->shqk", picked, seq_keys, preferred_element_type=jnp.float32
    ) * head_size ** (-0.5)
    key_position = jnp.arange(page_count * page_len, dtype=jnp.int32)
    last_key = cached[:, None] + slot_ids[None, :]
    allowed = key_position[None, None, :] <= last_key[:, :, None]
    scores = jnp.where(allowed[:, None, :, :], scores, -1e30)
    row_max = jnp.max(scores, axis=-1, keepdims=True)
    weights = jnp.exp(scores - row_max)
    row_total = jnp.sum(weights, axis=-1, keepdims=True)
    probabilities = weights.astype(jnp.bfloat16)
    attended = (
        jnp.einsum("shqk,skhd->shqd", probabilities, seq_values, preferred_element_type=jnp.float32)
        / row_total
    )
    attended = (
        attended.astype(jnp.bfloat16).transpose(0, 2, 1, 3).reshape(seq_count, QMAX, lane_count)
    )
    row_ids = jnp.arange(row_count, dtype=jnp.int32)
    owning = jnp.sum((starts[None, :] <= row_ids[:, None]).astype(jnp.int32), axis=1) - 1
    offset = row_ids - starts[owning]
    return attended[owning, offset]


def on_device(
    stream,
    queries,
    key_pages,
    value_pages,
    query_counts,
    cached_lengths,
    page_tables,
    out_proj,
    moe_gain,
    router,
    gate_proj,
    up_proj,
    down_proj,
    routes,
    next_gain,
):
    held = lax.all_gather(
        jnp.stack([gate_proj[0], up_proj[0], down_proj[0]]), "zz", axis=1, tiled=True
    )
    gate_held = held[0]
    up_held = held[1]
    down_held = held[2]
    heads_here = queries.shape[1] // HD
    attended = paged_attention(
        queries,
        key_pages,
        value_pages,
        query_counts[0],
        cached_lengths[0],
        page_tables[0],
        heads_here,
    )
    own_rows = stream.shape[0]
    partial_proj = jnp.dot(attended, out_proj, preferred_element_type=jnp.float32).astype(
        jnp.bfloat16
    )
    expert_count = lax.axis_size("expert")
    gathered_proj = lax.all_to_all(
        partial_proj.reshape(expert_count, own_rows, partial_proj.shape[1]),
        "expert",
        split_axis=0,
        concat_axis=0,
        tiled=True,
    )
    projected = jnp.sum(gathered_proj.astype(jnp.float32), axis=0)
    hidden = stream.astype(jnp.float32) + projected
    normed = rms_scale(hidden, moe_gain).astype(jnp.bfloat16)
    logits = jnp.dot(normed, router, preferred_element_type=jnp.float32)
    chosen = jnp.take_along_axis(logits, routes, axis=1)
    first_share = jax.nn.sigmoid(chosen[:, 0] - chosen[:, 1])
    shares = jnp.stack([first_share, 1.0 - first_share], axis=1)
    expert_devs = lax.axis_size("expert")
    experts_all = expert_devs // 2
    model_width = stream.shape[1]
    capacity = max(2, min(own_rows, 3 * own_rows // experts_all))
    flat_routes = routes.reshape(-1)
    onehot = (flat_routes[:, None] == jnp.arange(experts_all, dtype=jnp.int32)[None, :]).astype(
        jnp.int32
    )
    earlier = jnp.cumsum(onehot, axis=0) - onehot
    position = jnp.sum(earlier * onehot, axis=1)
    target = flat_routes * capacity + position
    placing = (
        jnp.arange(experts_all * capacity, dtype=jnp.int32)[:, None] == target[None, :]
    ).astype(jnp.bfloat16)
    repeated = jnp.repeat(normed, 2, axis=0)
    packed = jnp.dot(placing, repeated, preferred_element_type=jnp.float32).astype(jnp.bfloat16)
    packed = packed.reshape(experts_all, 1, capacity, model_width)
    outgoing = jnp.broadcast_to(packed, (experts_all, 2, capacity, model_width))
    arrived = lax.all_to_all(
        outgoing.reshape(expert_devs * capacity, model_width),
        "expert",
        split_axis=0,
        concat_axis=0,
        tiled=True,
    )
    n_zz = lax.axis_size("zz")
    n_h = lax.axis_size("h")
    n_c = lax.axis_size("c")
    slot_total = arrived.shape[0]
    piece = slot_total // n_zz
    sent = lax.all_to_all(
        arrived.reshape(n_zz, piece, model_width), "zz", split_axis=0, concat_axis=0, tiled=True
    )
    swap = [(0, 1), (1, 0)]
    from_h = lax.ppermute(sent, "h", swap)
    both_h = jnp.stack([sent, from_h])
    from_c = lax.ppermute(both_h, "c", swap)
    rows_here = jnp.stack([both_h, from_c])
    flat_rows = rows_here.reshape(n_c * n_h * n_zz * piece, model_width)
    gate_val = lax.dot_general(
        flat_rows, gate_held, (((1,), (1,)), ((), ())), preferred_element_type=jnp.float32
    )
    up_val = lax.dot_general(
        flat_rows, up_held, (((1,), (1,)), ((), ())), preferred_element_type=jnp.float32
    )
    activated = (jax.nn.silu(gate_val) * up_val).astype(jnp.bfloat16)
    partial = jnp.dot(activated, down_held, preferred_element_type=jnp.float32).astype(jnp.bfloat16)
    partial = partial.reshape(n_c, n_h, n_zz, piece, model_width)
    back_c = lax.ppermute(partial[1], "c", swap)
    sum_c = (partial[0].astype(jnp.float32) + back_c.astype(jnp.float32)).astype(jnp.bfloat16)
    by_dest = jnp.where(lax.axis_index("h") == 0, sum_c, sum_c[::-1]).transpose(1, 0, 2, 3)
    both_back = lax.all_to_all(
        by_dest.reshape(n_zz * n_h, piece, model_width),
        ("zz", "h"),
        split_axis=0,
        concat_axis=0,
        tiled=True,
    )
    own_slots = jnp.sum(
        both_back.reshape(n_zz, n_h, piece, model_width).astype(jnp.float32), axis=1
    ).astype(jnp.bfloat16)
    returned = lax.all_to_all(
        own_slots.reshape(slot_total, model_width), "expert", split_axis=0, concat_axis=0, tiled=True
    ).astype(jnp.float32)
    arranged = returned.reshape(experts_all, 2, capacity, model_width)
    expert_result = jnp.sum(arranged, axis=1)
    per_slot = expert_result.reshape(experts_all * capacity, model_width)[target]
    expert_mix = jnp.sum(per_slot.reshape(own_rows, 2, model_width) * shares[:, :, None], axis=1)
    combined = hidden + expert_mix
    return (combined.astype(jnp.bfloat16), rms_scale(combined, next_gain).astype(jnp.bfloat16))


def solution(mesh):
    n_dp = mesh.shape["dp"]
    n_chips = n_dp // 2
    split = jax.sharding.Mesh(
        mesh.devices.reshape(n_chips // 2, 2, 2, mesh.shape["expert"]), ("zz", "h", "c", "expert")
    )
    dp = ("zz", "h", "c")
    placed = (
        P((*dp, "expert"), None),
        P(dp, "expert"),
        P(dp, None, "expert"),
        P(dp, None, "expert"),
        P(dp, None),
        P(dp, None),
        P(dp, None),
        P("expert", None),
        P(),
        P(),
        P("expert", dp, None),
        P("expert", dp, None),
        P("expert", dp, None),
        P((*dp, "expert"), None),
        P(),
    )

    return jax.shard_map(
        on_device,
        mesh=split,
        in_specs=placed,
        out_specs=(P((*dp, "expert"), None), P((*dp, "expert"), None)),
        check_vma=False,
    )
```

```python
import jax
import jax.numpy as jnp
from jax import lax
from jax.sharding import PartitionSpec as P

HD = 64
QMAX = 32


eps = 1e-06


def rms_scale(values, gain):
    mean_square = jnp.mean(values * values, axis=-1, keepdims=True)
    return values * lax.rsqrt(mean_square + eps) * gain


def paged_attention(
    group_queries, group_keys, group_values, counts, cached, page_table, head_count
):
    row_count, lane_count = group_queries.shape
    head_size = lane_count // head_count
    seq_count = counts.shape[0]
    page_count = page_table.shape[0] // seq_count
    page_len = group_keys.shape[1]
    starts = jnp.cumsum(counts) - counts
    slot_ids = jnp.arange(QMAX, dtype=jnp.int32)
    row_index = jnp.clip(starts[:, None] + slot_ids[None, :], 0, row_count - 1)
    picked = group_queries[row_index].reshape(seq_count, QMAX, head_count, head_size)
    page_ids = page_table.reshape(seq_count, page_count)
    seq_keys = group_keys[page_ids].reshape(seq_count, page_count * page_len, head_count, head_size)
    seq_values = group_values[page_ids].reshape(
        seq_count, page_count * page_len, head_count, head_size
    )
    scores = jnp.einsum(
        "sqhd,skhd->shqk", picked, seq_keys, preferred_element_type=jnp.float32
    ) * head_size ** (-0.5)
    key_position = jnp.arange(page_count * page_len, dtype=jnp.int32)
    last_key = cached[:, None] + slot_ids[None, :]
    allowed = key_position[None, None, :] <= last_key[:, :, None]
    scores = jnp.where(allowed[:, None, :, :], scores, -1e30)
    row_max = jnp.max(scores, axis=-1, keepdims=True)
    weights = jnp.exp(scores - row_max)
    row_total = jnp.sum(weights, axis=-1, keepdims=True)
    probabilities = weights.astype(jnp.bfloat16)
    attended = (
        jnp.einsum("shqk,skhd->shqd", probabilities, seq_values, preferred_element_type=jnp.float32)
        / row_total
    )
    attended = (
        attended.astype(jnp.bfloat16).transpose(0, 2, 1, 3).reshape(seq_count, QMAX, lane_count)
    )
    row_ids = jnp.arange(row_count, dtype=jnp.int32)
    owning = jnp.sum((starts[None, :] <= row_ids[:, None]).astype(jnp.int32), axis=1) - 1
    offset = row_ids - starts[owning]
    return attended[owning, offset]


def on_device(
    stream,
    queries,
    key_pages,
    value_pages,
    query_counts,
    cached_lengths,
    page_tables,
    out_proj,
    moe_gain,
    router,
    gate_proj,
    up_proj,
    down_proj,
    routes,
    next_gain,
):
    held = lax.all_gather(
        jnp.stack([gate_proj[0], up_proj[0], down_proj[0]]), "zz", axis=1, tiled=True
    )
    gate_held = held[0]
    down_held = held[2]
    heads_here = queries.shape[1] // HD
    attended = paged_attention(
        queries,
        key_pages,
        value_pages,
        query_counts[0],
        cached_lengths[0],
        page_tables[0],
        heads_here,
    )
    own_rows = stream.shape[0]
    partial_proj = jnp.dot(attended, out_proj, preferred_element_type=jnp.float32).astype(
        jnp.bfloat16
    )
    expert_count = lax.axis_size("expert")
    gathered_proj = lax.all_to_all(
        partial_proj.reshape(expert_count, own_rows, partial_proj.shape[1]),
        "expert",
        split_axis=0,
        concat_axis=0,
        tiled=True,
    )
    projected = jnp.sum(gathered_proj.astype(jnp.float32), axis=0)
    hidden = stream.astype(jnp.float32) + projected
    normed = rms_scale(hidden, moe_gain).astype(jnp.bfloat16)
    logits = jnp.dot(normed, router, preferred_element_type=jnp.float32)
    chosen = jnp.take_along_axis(logits, routes, axis=1)
    first_share = jax.nn.sigmoid(chosen[:, 0] - chosen[:, 1])
    shares = jnp.stack([first_share, 1.0 - first_share], axis=1)
    expert_devs = lax.axis_size("expert")
    experts_all = expert_devs // 2
    model_width = stream.shape[1]
    capacity = max(2, min(own_rows, 3 * own_rows // experts_all))
    flat_routes = routes.reshape(-1)
    onehot = (flat_routes[:, None] == jnp.arange(experts_all, dtype=jnp.int32)[None, :]).astype(
        jnp.int32
    )
    earlier = jnp.cumsum(onehot, axis=0) - onehot
    position = jnp.sum(earlier * onehot, axis=1)
    target = flat_routes * capacity + position
    placing = (
        jnp.arange(experts_all * capacity, dtype=jnp.int32)[:, None] == target[None, :]
    ).astype(jnp.bfloat16)
    repeated = jnp.repeat(normed, 2, axis=0)
    packed = jnp.dot(placing, repeated, preferred_element_type=jnp.float32).astype(jnp.bfloat16)
    packed = packed.reshape(experts_all, 1, capacity, model_width)
    outgoing = jnp.broadcast_to(packed, (experts_all, 2, capacity, model_width))
    arrived = lax.all_to_all(
        outgoing.reshape(expert_devs * capacity, model_width),
        "expert",
        split_axis=0,
        concat_axis=0,
        tiled=True,
    )
    n_zz = lax.axis_size("zz")
    slot_total = arrived.shape[0]
    piece = slot_total // n_zz
    sent = lax.all_to_all(
        arrived.reshape(n_zz, piece, model_width), "zz", split_axis=0, concat_axis=0, tiled=True
    )
    swap = [(0, 1), (1, 0)]
    from_h = lax.ppermute(sent, "h", swap)
    both_h = jnp.stack([sent, from_h])
    from_c = lax.ppermute(both_h, "c", swap)
    rows_here = jnp.stack([both_h, from_c])
    gate_up = held[:2].reshape(-1, model_width)
    units = gate_held.shape[0]

    def expert_part(rows):
        flat_rows = rows.reshape(-1, model_width)
        both = lax.dot_general(
            flat_rows, gate_up, (((1,), (1,)), ((), ())), preferred_element_type=jnp.float32
        )
        activated = (jax.nn.silu(both[:, :units]) * both[:, units:]).astype(jnp.bfloat16)
        part = jnp.dot(activated, down_held, preferred_element_type=jnp.float32)
        return part.astype(jnp.bfloat16).reshape(rows.shape)

    other_core = expert_part(rows_here[1])
    back_c = lax.ppermute(other_core, "c", swap)
    other_block = expert_part(rows_here[0, 1])
    sum_other = (other_block.astype(jnp.float32) + back_c[1].astype(jnp.float32)).astype(
        jnp.bfloat16
    )
    back_h = lax.ppermute(sum_other, "h", swap)
    own = expert_part(rows_here[0, 0])
    sum_own = (own.astype(jnp.float32) + back_c[0].astype(jnp.float32)).astype(jnp.bfloat16)
    summed = (sum_own.astype(jnp.float32) + back_h.astype(jnp.float32)).astype(jnp.bfloat16)
    own_slots = lax.all_to_all(summed, "zz", split_axis=0, concat_axis=0, tiled=True)
    returned = lax.all_to_all(
        own_slots.reshape(slot_total, model_width), "expert", split_axis=0, concat_axis=0, tiled=True
    ).astype(jnp.float32)
    arranged = returned.reshape(experts_all, 2, capacity, model_width)
    expert_result = jnp.sum(arranged, axis=1)
    per_slot = expert_result.reshape(experts_all * capacity, model_width)[target]
    expert_mix = jnp.sum(per_slot.reshape(own_rows, 2, model_width) * shares[:, :, None], axis=1)
    combined = hidden + expert_mix
    return (combined.astype(jnp.bfloat16), rms_scale(combined, next_gain).astype(jnp.bfloat16))


def solution(mesh):
    n_dp = mesh.shape["dp"]
    n_chips = n_dp // 2
    split = jax.sharding.Mesh(
        mesh.devices.reshape(n_chips // 2, 2, 2, mesh.shape["expert"]), ("zz", "h", "c", "expert")
    )
    dp = ("zz", "h", "c")
    placed = (
        P((*dp, "expert"), None),
        P(dp, "expert"),
        P(dp, None, "expert"),
        P(dp, None, "expert"),
        P(dp, None),
        P(dp, None),
        P(dp, None),
        P("expert", None),
        P(),
        P(),
        P("expert", dp, None),
        P("expert", dp, None),
        P("expert", dp, None),
        P((*dp, "expert"), None),
        P(),
    )

    return jax.shard_map(
        on_device,
        mesh=split,
        in_specs=placed,
        out_specs=(P((*dp, "expert"), None), P((*dp, "expert"), None)),
        check_vma=False,
    )
```

```python
import jax
import jax.numpy as jnp
from jax import lax
from jax.sharding import PartitionSpec as P

HD = 64
QMAX = 32


eps = 1e-06


def rms_scale(values, gain):
    mean_square = jnp.mean(values * values, axis=-1, keepdims=True)
    return values * lax.rsqrt(mean_square + eps) * gain


def paged_attention(
    group_queries, group_keys, group_values, counts, cached, page_table, head_count
):
    row_count, lane_count = group_queries.shape
    head_size = lane_count // head_count
    seq_count = counts.shape[0]
    page_count = page_table.shape[0] // seq_count
    page_len = group_keys.shape[1]
    starts = jnp.cumsum(counts) - counts
    slot_ids = jnp.arange(QMAX, dtype=jnp.int32)
    row_index = jnp.clip(starts[:, None] + slot_ids[None, :], 0, row_count - 1)
    picked = group_queries[row_index].reshape(seq_count, QMAX, head_count, head_size)
    page_ids = page_table.reshape(seq_count, page_count)
    seq_keys = group_keys[page_ids].reshape(seq_count, page_count * page_len, head_count, head_size)
    seq_values = group_values[page_ids].reshape(
        seq_count, page_count * page_len, head_count, head_size
    )
    scores = jnp.einsum(
        "sqhd,skhd->shqk", picked, seq_keys, preferred_element_type=jnp.float32
    ) * head_size ** (-0.5)
    key_position = jnp.arange(page_count * page_len, dtype=jnp.int32)
    last_key = cached[:, None] + slot_ids[None, :]
    allowed = key_position[None, None, :] <= last_key[:, :, None]
    scores = jnp.where(allowed[:, None, :, :], scores, -1e30)
    row_max = jnp.max(scores, axis=-1, keepdims=True)
    weights = jnp.exp(scores - row_max)
    row_total = jnp.sum(weights, axis=-1, keepdims=True)
    probabilities = weights.astype(jnp.bfloat16)
    attended = (
        jnp.einsum("shqk,skhd->shqd", probabilities, seq_values, preferred_element_type=jnp.float32)
        / row_total
    )
    attended = (
        attended.astype(jnp.bfloat16).transpose(0, 2, 1, 3).reshape(seq_count, QMAX, lane_count)
    )
    row_ids = jnp.arange(row_count, dtype=jnp.int32)
    owning = jnp.sum((starts[None, :] <= row_ids[:, None]).astype(jnp.int32), axis=1) - 1
    offset = row_ids - starts[owning]
    return attended[owning, offset]


def on_device(
    stream,
    queries,
    key_pages,
    value_pages,
    query_counts,
    cached_lengths,
    page_tables,
    out_proj,
    moe_gain,
    router,
    gate_proj,
    up_proj,
    down_proj,
    routes,
    next_gain,
):
    held = lax.all_gather(
        jnp.stack([gate_proj[0], up_proj[0], down_proj[0]]), "zz", axis=1, tiled=True
    )
    gate_held = held[0]
    up_held = held[1]
    down_held = held[2]
    heads_here = queries.shape[1] // HD
    attended = paged_attention(
        queries,
        key_pages,
        value_pages,
        query_counts[0],
        cached_lengths[0],
        page_tables[0],
        heads_here,
    )
    own_rows = stream.shape[0]
    partial_proj = jnp.dot(attended, out_proj, preferred_element_type=jnp.float32).astype(
        jnp.bfloat16
    )
    expert_count = lax.axis_size("expert")
    gathered_proj = lax.all_to_all(
        partial_proj.reshape(expert_count, own_rows, partial_proj.shape[1]),
        "expert",
        split_axis=0,
        concat_axis=0,
        tiled=True,
    )
    projected = jnp.sum(gathered_proj.astype(jnp.float32), axis=0)
    hidden = stream.astype(jnp.float32) + projected
    normed = rms_scale(hidden, moe_gain).astype(jnp.bfloat16)
    logits = jnp.dot(normed, router, preferred_element_type=jnp.float32)
    chosen = jnp.take_along_axis(logits, routes, axis=1)
    first_share = jax.nn.sigmoid(chosen[:, 0] - chosen[:, 1])
    shares = jnp.stack([first_share, 1.0 - first_share], axis=1)
    expert_devs = lax.axis_size("expert")
    experts_all = expert_devs // 2
    model_width = stream.shape[1]
    capacity = max(2, min(own_rows, 3 * own_rows // experts_all))
    flat_routes = routes.reshape(-1)
    onehot = (flat_routes[:, None] == jnp.arange(experts_all, dtype=jnp.int32)[None, :]).astype(
        jnp.int32
    )
    earlier = jnp.cumsum(onehot, axis=0) - onehot
    position = jnp.sum(earlier * onehot, axis=1)
    target = flat_routes * capacity + position
    placing = (
        jnp.arange(experts_all * capacity, dtype=jnp.int32)[:, None] == target[None, :]
    ).astype(jnp.bfloat16)
    repeated = jnp.repeat(normed, 2, axis=0)
    packed = jnp.dot(placing, repeated, preferred_element_type=jnp.float32).astype(jnp.bfloat16)
    packed = packed.reshape(experts_all, 1, capacity, model_width)
    outgoing = jnp.broadcast_to(packed, (experts_all, 2, capacity, model_width))
    arrived = lax.all_to_all(
        outgoing.reshape(expert_devs * capacity, model_width),
        "expert",
        split_axis=0,
        concat_axis=0,
        tiled=True,
    )
    n_zz = lax.axis_size("zz")
    n_h = lax.axis_size("h")
    n_c = lax.axis_size("c")
    slot_total = arrived.shape[0]
    piece = slot_total // n_zz
    half_cap = capacity // 2
    column_odd = lax.axis_index("expert") % 2
    by_piece = arrived.reshape(n_zz, 2, capacity, model_width)
    mine = lax.dynamic_slice_in_dim(by_piece, column_odd * half_cap, half_cap, axis=2)
    sent = lax.all_to_all(
        mine.reshape(n_zz, piece // 2, model_width), "zz", split_axis=0, concat_axis=0, tiled=True
    )
    swap = [(0, 1), (1, 0)]
    from_h = lax.ppermute(sent, "h", swap)
    both_h = jnp.stack([sent, from_h])
    from_c = lax.ppermute(both_h, "c", swap)
    half_rows = jnp.stack([both_h, from_c]).reshape(n_c, n_h, n_zz, 2, half_cap, model_width)
    other_half = lax.ppermute(
        half_rows, "expert", [(i, i ^ 1) for i in range(expert_devs)]
    )
    rows_here = jnp.where(
        column_odd == 0,
        jnp.concatenate([half_rows, other_half], axis=4),
        jnp.concatenate([other_half, half_rows], axis=4),
    ).reshape(n_c, n_h, n_zz, piece, model_width)
    flat_rows = rows_here.reshape(n_c * n_h * n_zz * piece, model_width)
    gate_val = lax.dot_general(
        flat_rows, gate_held, (((1,), (1,)), ((), ())), preferred_element_type=jnp.float32
    )
    up_val = lax.dot_general(
        flat_rows, up_held, (((1,), (1,)), ((), ())), preferred_element_type=jnp.float32
    )
    activated = (jax.nn.silu(gate_val) * up_val).astype(jnp.bfloat16)
    partial = jnp.dot(activated, down_held, preferred_element_type=jnp.float32).astype(jnp.bfloat16)
    partial = partial.reshape(n_c, n_h, n_zz, piece, model_width)
    back_c = lax.ppermute(partial[1], "c", swap)
    sum_c = (partial[0].astype(jnp.float32) + back_c.astype(jnp.float32)).astype(jnp.bfloat16)
    back_h = lax.ppermute(sum_c[1], "h", swap)
    summed = (sum_c[0].astype(jnp.float32) + back_h.astype(jnp.float32)).astype(jnp.bfloat16)
    own_slots = lax.all_to_all(summed, "zz", split_axis=0, concat_axis=0, tiled=True)
    returned = lax.all_to_all(
        own_slots.reshape(slot_total, model_width), "expert", split_axis=0, concat_axis=0, tiled=True
    ).astype(jnp.float32)
    arranged = returned.reshape(experts_all, 2, capacity, model_width)
    expert_result = jnp.sum(arranged, axis=1)
    per_slot = expert_result.reshape(experts_all * capacity, model_width)[target]
    expert_mix = jnp.sum(per_slot.reshape(own_rows, 2, model_width) * shares[:, :, None], axis=1)
    combined = hidden + expert_mix
    return (combined.astype(jnp.bfloat16), rms_scale(combined, next_gain).astype(jnp.bfloat16))


def solution(mesh):
    n_dp = mesh.shape["dp"]
    n_chips = n_dp // 2
    split = jax.sharding.Mesh(
        mesh.devices.reshape(n_chips // 2, 2, 2, mesh.shape["expert"]), ("zz", "h", "c", "expert")
    )
    dp = ("zz", "h", "c")
    placed = (
        P((*dp, "expert"), None),
        P(dp, "expert"),
        P(dp, None, "expert"),
        P(dp, None, "expert"),
        P(dp, None),
        P(dp, None),
        P(dp, None),
        P("expert", None),
        P(),
        P(),
        P("expert", dp, None),
        P("expert", dp, None),
        P("expert", dp, None),
        P((*dp, "expert"), None),
        P(),
    )

    return jax.shard_map(
        on_device,
        mesh=split,
        in_specs=placed,
        out_specs=(P((*dp, "expert"), None), P((*dp, "expert"), None)),
        check_vma=False,
    )
```

```python
import jax
import jax.numpy as jnp
from jax import lax
from jax.sharding import PartitionSpec as P

HD = 64
QMAX = 32


eps = 1e-06


def rms_scale(values, gain):
    mean_square = jnp.mean(values * values, axis=-1, keepdims=True)
    return values * lax.rsqrt(mean_square + eps) * gain


def paged_attention(
    group_queries, group_keys, group_values, counts, cached, page_table, head_count
):
    row_count, lane_count = group_queries.shape
    head_size = lane_count // head_count
    seq_count = counts.shape[0]
    page_count = page_table.shape[0] // seq_count
    page_len = group_keys.shape[1]
    starts = jnp.cumsum(counts) - counts
    slot_ids = jnp.arange(QMAX, dtype=jnp.int32)
    row_index = jnp.clip(starts[:, None] + slot_ids[None, :], 0, row_count - 1)
    picked = group_queries[row_index].reshape(seq_count, QMAX, head_count, head_size)
    page_ids = page_table.reshape(seq_count, page_count)
    seq_keys = group_keys[page_ids].reshape(seq_count, page_count * page_len, head_count, head_size)
    seq_values = group_values[page_ids].reshape(
        seq_count, page_count * page_len, head_count, head_size
    )
    scores = jnp.einsum(
        "sqhd,skhd->shqk", picked, seq_keys, preferred_element_type=jnp.float32
    ) * head_size ** (-0.5)
    key_position = jnp.arange(page_count * page_len, dtype=jnp.int32)
    last_key = cached[:, None] + slot_ids[None, :]
    allowed = key_position[None, None, :] <= last_key[:, :, None]
    scores = jnp.where(allowed[:, None, :, :], scores, -1e30)
    row_max = jnp.max(scores, axis=-1, keepdims=True)
    weights = jnp.exp(scores - row_max)
    row_total = jnp.sum(weights, axis=-1, keepdims=True)
    probabilities = weights.astype(jnp.bfloat16)
    attended = (
        jnp.einsum("shqk,skhd->shqd", probabilities, seq_values, preferred_element_type=jnp.float32)
        / row_total
    )
    attended = (
        attended.astype(jnp.bfloat16).transpose(0, 2, 1, 3).reshape(seq_count, QMAX, lane_count)
    )
    row_ids = jnp.arange(row_count, dtype=jnp.int32)
    owning = jnp.sum((starts[None, :] <= row_ids[:, None]).astype(jnp.int32), axis=1) - 1
    offset = row_ids - starts[owning]
    return attended[owning, offset]


def on_device(
    stream,
    queries,
    key_pages,
    value_pages,
    query_counts,
    cached_lengths,
    page_tables,
    out_proj,
    moe_gain,
    router,
    gate_proj,
    up_proj,
    down_proj,
    routes,
    next_gain,
):
    held = lax.all_gather(
        jnp.stack([gate_proj[0], up_proj[0], down_proj[0]]), "zz", axis=1, tiled=True
    )
    gate_held = held[0]
    up_held = held[1]
    down_held = held[2]
    heads_here = queries.shape[1] // HD
    attended = paged_attention(
        queries,
        key_pages,
        value_pages,
        query_counts[0],
        cached_lengths[0],
        page_tables[0],
        heads_here,
    )
    own_rows = stream.shape[0]
    partial_proj = jnp.dot(attended, out_proj, preferred_element_type=jnp.float32).astype(
        jnp.bfloat16
    )
    expert_count = lax.axis_size("expert")
    gathered_proj = lax.all_to_all(
        partial_proj.reshape(expert_count, own_rows, partial_proj.shape[1]),
        "expert",
        split_axis=0,
        concat_axis=0,
        tiled=True,
    )
    projected = jnp.sum(gathered_proj.astype(jnp.float32), axis=0)
    hidden = stream.astype(jnp.float32) + projected
    normed = rms_scale(hidden, moe_gain).astype(jnp.bfloat16)
    logits = jnp.dot(normed, router, preferred_element_type=jnp.float32)
    chosen = jnp.take_along_axis(logits, routes, axis=1)
    first_share = jax.nn.sigmoid(chosen[:, 0] - chosen[:, 1])
    shares = jnp.stack([first_share, 1.0 - first_share], axis=1)
    expert_devs = lax.axis_size("expert")
    experts_all = expert_devs // 2
    model_width = stream.shape[1]
    capacity = max(2, min(own_rows, 3 * own_rows // experts_all))
    flat_routes = routes.reshape(-1)
    onehot = (flat_routes[:, None] == jnp.arange(experts_all, dtype=jnp.int32)[None, :]).astype(
        jnp.int32
    )
    earlier = jnp.cumsum(onehot, axis=0) - onehot
    position = jnp.sum(earlier * onehot, axis=1)
    target = flat_routes * capacity + position
    placing = (
        jnp.arange(experts_all * capacity, dtype=jnp.int32)[:, None] == target[None, :]
    ).astype(jnp.bfloat16)
    repeated = jnp.repeat(normed, 2, axis=0)
    packed = jnp.dot(placing, repeated, preferred_element_type=jnp.float32).astype(jnp.bfloat16)
    packed = packed.reshape(experts_all, 1, capacity, model_width)
    outgoing = jnp.broadcast_to(packed, (experts_all, 2, capacity, model_width))
    arrived = lax.all_to_all(
        outgoing.reshape(expert_devs * capacity, model_width),
        "expert",
        split_axis=0,
        concat_axis=0,
        tiled=True,
    )
    n_zz = lax.axis_size("zz")
    n_h = lax.axis_size("h")
    n_c = lax.axis_size("c")
    slot_total = arrived.shape[0]
    piece = slot_total // n_zz
    half_cap = capacity // 2
    column_odd = lax.axis_index("expert") % 2
    by_piece = arrived.reshape(n_zz, 2, capacity, model_width)
    mine = lax.dynamic_slice_in_dim(by_piece, column_odd * half_cap, half_cap, axis=2)
    sent = lax.all_to_all(
        mine.reshape(n_zz, piece // 2, model_width), "zz", split_axis=0, concat_axis=0, tiled=True
    )
    swap = [(0, 1), (1, 0)]
    from_h = lax.ppermute(sent, "h", swap)
    both_h = jnp.stack([sent, from_h])
    from_c = lax.ppermute(both_h, "c", swap)
    half_rows = jnp.stack([both_h, from_c]).reshape(n_c, n_h, n_zz, 2, half_cap, model_width)
    other_half = lax.ppermute(
        half_rows, "expert", [(i, i ^ 1) for i in range(expert_devs)]
    )
    rows_here = jnp.where(
        column_odd == 0,
        jnp.concatenate([half_rows, other_half], axis=4),
        jnp.concatenate([other_half, half_rows], axis=4),
    ).reshape(n_c, n_h, n_zz, piece, model_width)
    flat_rows = rows_here.reshape(n_c * n_h * n_zz * piece, model_width)
    gate_val = lax.dot_general(
        flat_rows, gate_held, (((1,), (1,)), ((), ())), preferred_element_type=jnp.float32
    )
    up_val = lax.dot_general(
        flat_rows, up_held, (((1,), (1,)), ((), ())), preferred_element_type=jnp.float32
    )
    activated = (jax.nn.silu(gate_val) * up_val).astype(jnp.bfloat16)
    partial = jnp.dot(activated, down_held, preferred_element_type=jnp.float32).astype(jnp.bfloat16)
    partial = partial.reshape(n_c, n_h, n_zz, piece, model_width)
    back_c = lax.ppermute(partial[1], "c", swap)
    sum_c = (partial[0].astype(jnp.float32) + back_c.astype(jnp.float32)).astype(jnp.bfloat16)
    back_h = lax.ppermute(sum_c[1], "h", swap)
    summed = (sum_c[0].astype(jnp.float32) + back_h.astype(jnp.float32)).astype(jnp.bfloat16)
    by_half = summed.reshape(n_zz, 2, 2, half_cap, model_width)
    keep = lax.dynamic_index_in_dim(by_half, column_odd, axis=2, keepdims=False)
    give = lax.dynamic_index_in_dim(by_half, 1 - column_odd, axis=2, keepdims=False)
    taken = lax.ppermute(give, "expert", [(i, i ^ 1) for i in range(expert_devs)])
    both_columns = (keep.astype(jnp.float32) + taken.astype(jnp.float32)).astype(jnp.bfloat16)
    own_slots = lax.all_to_all(
        both_columns.reshape(n_zz, piece // 2, model_width), "zz", split_axis=0, concat_axis=0, tiled=True
    )
    returned = lax.all_to_all(
        own_slots.reshape(expert_devs, half_cap, model_width), "expert", split_axis=0, concat_axis=0, tiled=True
    ).astype(jnp.float32)
    expert_result = returned.reshape(experts_all, capacity, model_width)
    per_slot = expert_result.reshape(experts_all * capacity, model_width)[target]
    expert_mix = jnp.sum(per_slot.reshape(own_rows, 2, model_width) * shares[:, :, None], axis=1)
    combined = hidden + expert_mix
    return (combined.astype(jnp.bfloat16), rms_scale(combined, next_gain).astype(jnp.bfloat16))


def solution(mesh):
    n_dp = mesh.shape["dp"]
    n_chips = n_dp // 2
    split = jax.sharding.Mesh(
        mesh.devices.reshape(n_chips // 2, 2, 2, mesh.shape["expert"]), ("zz", "h", "c", "expert")
    )
    dp = ("zz", "h", "c")
    placed = (
        P((*dp, "expert"), None),
        P(dp, "expert"),
        P(dp, None, "expert"),
        P(dp, None, "expert"),
        P(dp, None),
        P(dp, None),
        P(dp, None),
        P("expert", None),
        P(),
        P(),
        P("expert", dp, None),
        P("expert", dp, None),
        P("expert", dp, None),
        P((*dp, "expert"), None),
        P(),
    )

    return jax.shard_map(
        on_device,
        mesh=split,
        in_specs=placed,
        out_specs=(P((*dp, "expert"), None), P((*dp, "expert"), None)),
        check_vma=False,
    )
```

```python
import jax
import jax.numpy as jnp
from jax import lax
from jax.sharding import PartitionSpec as P

HD = 64
QMAX = 32


eps = 1e-06


def rms_scale(values, gain):
    mean_square = jnp.mean(values * values, axis=-1, keepdims=True)
    return values * lax.rsqrt(mean_square + eps) * gain


def paged_attention(
    group_queries, group_keys, group_values, counts, cached, page_table, head_count
):
    row_count, lane_count = group_queries.shape
    head_size = lane_count // head_count
    seq_count = counts.shape[0]
    page_count = page_table.shape[0] // seq_count
    page_len = group_keys.shape[1]
    starts = jnp.cumsum(counts) - counts
    slot_ids = jnp.arange(QMAX, dtype=jnp.int32)
    row_index = jnp.clip(starts[:, None] + slot_ids[None, :], 0, row_count - 1)
    picked = group_queries[row_index].reshape(seq_count, QMAX, head_count, head_size)
    page_ids = page_table.reshape(seq_count, page_count)
    seq_keys = group_keys[page_ids].reshape(seq_count, page_count * page_len, head_count, head_size)
    seq_values = group_values[page_ids].reshape(
        seq_count, page_count * page_len, head_count, head_size
    )
    scores = jnp.einsum(
        "sqhd,skhd->shqk", picked, seq_keys, preferred_element_type=jnp.float32
    ) * head_size ** (-0.5)
    key_position = jnp.arange(page_count * page_len, dtype=jnp.int32)
    last_key = cached[:, None] + slot_ids[None, :]
    allowed = key_position[None, None, :] <= last_key[:, :, None]
    scores = jnp.where(allowed[:, None, :, :], scores, -1e30)
    row_max = jnp.max(scores, axis=-1, keepdims=True)
    weights = jnp.exp(scores - row_max)
    row_total = jnp.sum(weights, axis=-1, keepdims=True)
    probabilities = weights.astype(jnp.bfloat16)
    attended = (
        jnp.einsum("shqk,skhd->shqd", probabilities, seq_values, preferred_element_type=jnp.float32)
        / row_total
    )
    attended = (
        attended.astype(jnp.bfloat16).transpose(0, 2, 1, 3).reshape(seq_count, QMAX, lane_count)
    )
    row_ids = jnp.arange(row_count, dtype=jnp.int32)
    owning = jnp.sum((starts[None, :] <= row_ids[:, None]).astype(jnp.int32), axis=1) - 1
    offset = row_ids - starts[owning]
    return attended[owning, offset]


def on_device(
    stream,
    queries,
    key_pages,
    value_pages,
    query_counts,
    cached_lengths,
    page_tables,
    out_proj,
    moe_gain,
    router,
    gate_proj,
    up_proj,
    down_proj,
    routes,
    next_gain,
):
    held = lax.all_gather(
        jnp.stack([gate_proj[0], up_proj[0], down_proj[0]]), "zz", axis=1, tiled=True
    )
    gate_held = held[0]
    up_held = held[1]
    down_held = held[2]
    heads_here = queries.shape[1] // HD
    attended = paged_attention(
        queries,
        key_pages,
        value_pages,
        query_counts[0],
        cached_lengths[0],
        page_tables[0],
        heads_here,
    )
    own_rows = stream.shape[0]
    partial_proj = jnp.dot(attended, out_proj, preferred_element_type=jnp.float32).astype(
        jnp.bfloat16
    )
    expert_count = lax.axis_size("expert")
    gathered_proj = lax.all_to_all(
        partial_proj.reshape(expert_count, own_rows, partial_proj.shape[1]),
        "expert",
        split_axis=0,
        concat_axis=0,
        tiled=True,
    )
    projected = jnp.sum(gathered_proj.astype(jnp.float32), axis=0)
    hidden = stream.astype(jnp.float32) + projected
    normed = rms_scale(hidden, moe_gain).astype(jnp.bfloat16)
    logits = jnp.dot(normed, router, preferred_element_type=jnp.float32)
    chosen = jnp.take_along_axis(logits, routes, axis=1)
    first_share = jax.nn.sigmoid(chosen[:, 0] - chosen[:, 1])
    shares = jnp.stack([first_share, 1.0 - first_share], axis=1)
    expert_devs = lax.axis_size("expert")
    experts_all = expert_devs // 2
    model_width = stream.shape[1]
    capacity = max(2, min(own_rows, 3 * own_rows // experts_all))
    flat_routes = routes.reshape(-1)
    onehot = (flat_routes[:, None] == jnp.arange(experts_all, dtype=jnp.int32)[None, :]).astype(
        jnp.int32
    )
    earlier = jnp.cumsum(onehot, axis=0) - onehot
    position = jnp.sum(earlier * onehot, axis=1)
    target = flat_routes * capacity + position
    placing = (
        jnp.arange(experts_all * capacity, dtype=jnp.int32)[:, None] == target[None, :]
    ).astype(jnp.bfloat16)
    repeated = jnp.repeat(normed, 2, axis=0)
    packed = jnp.dot(placing, repeated, preferred_element_type=jnp.float32).astype(jnp.bfloat16)
    arrived = lax.all_to_all(
        packed.reshape(expert_devs * (capacity // 2), model_width),
        "expert",
        split_axis=0,
        concat_axis=0,
        tiled=True,
    )
    n_zz = lax.axis_size("zz")
    n_h = lax.axis_size("h")
    n_c = lax.axis_size("c")
    slot_total = 2 * arrived.shape[0]
    piece = slot_total // n_zz
    half_cap = capacity // 2
    column_odd = lax.axis_index("expert") % 2
    mine = arrived.reshape(n_zz, 2, half_cap, model_width)
    sent = lax.all_to_all(
        mine.reshape(n_zz, piece // 2, model_width), "zz", split_axis=0, concat_axis=0, tiled=True
    )
    swap = [(0, 1), (1, 0)]
    from_h = lax.ppermute(sent, "h", swap)
    both_h = jnp.stack([sent, from_h])
    from_c = lax.ppermute(both_h, "c", swap)
    half_rows = jnp.stack([both_h, from_c]).reshape(n_c, n_h, n_zz, 2, half_cap, model_width)
    other_half = lax.ppermute(
        half_rows, "expert", [(i, i ^ 1) for i in range(expert_devs)]
    )
    rows_here = jnp.where(
        column_odd == 0,
        jnp.concatenate([half_rows, other_half], axis=4),
        jnp.concatenate([other_half, half_rows], axis=4),
    ).reshape(n_c, n_h, n_zz, piece, model_width)
    flat_rows = rows_here.reshape(n_c * n_h * n_zz * piece, model_width)
    gate_val = lax.dot_general(
        flat_rows, gate_held, (((1,), (1,)), ((), ())), preferred_element_type=jnp.float32
    )
    up_val = lax.dot_general(
        flat_rows, up_held, (((1,), (1,)), ((), ())), preferred_element_type=jnp.float32
    )
    activated = (jax.nn.silu(gate_val) * up_val).astype(jnp.bfloat16)
    partial = jnp.dot(activated, down_held, preferred_element_type=jnp.float32).astype(jnp.bfloat16)
    partial = partial.reshape(n_c, n_h, n_zz, piece, model_width)
    back_c = lax.ppermute(partial[1], "c", swap)
    sum_c = (partial[0].astype(jnp.float32) + back_c.astype(jnp.float32)).astype(jnp.bfloat16)
    back_h = lax.ppermute(sum_c[1], "h", swap)
    summed = (sum_c[0].astype(jnp.float32) + back_h.astype(jnp.float32)).astype(jnp.bfloat16)
    by_half = summed.reshape(n_zz, 2, 2, half_cap, model_width)
    keep = lax.dynamic_index_in_dim(by_half, column_odd, axis=2, keepdims=False)
    give = lax.dynamic_index_in_dim(by_half, 1 - column_odd, axis=2, keepdims=False)
    taken = lax.ppermute(give, "expert", [(i, i ^ 1) for i in range(expert_devs)])
    both_columns = (keep.astype(jnp.float32) + taken.astype(jnp.float32)).astype(jnp.bfloat16)
    own_slots = lax.all_to_all(
        both_columns.reshape(n_zz, piece // 2, model_width), "zz", split_axis=0, concat_axis=0, tiled=True
    )
    returned = lax.all_to_all(
        own_slots.reshape(expert_devs, half_cap, model_width), "expert", split_axis=0, concat_axis=0, tiled=True
    ).astype(jnp.float32)
    expert_result = returned.reshape(experts_all, capacity, model_width)
    per_slot = expert_result.reshape(experts_all * capacity, model_width)[target]
    expert_mix = jnp.sum(per_slot.reshape(own_rows, 2, model_width) * shares[:, :, None], axis=1)
    combined = hidden + expert_mix
    return (combined.astype(jnp.bfloat16), rms_scale(combined, next_gain).astype(jnp.bfloat16))


def solution(mesh):
    n_dp = mesh.shape["dp"]
    n_chips = n_dp // 2
    split = jax.sharding.Mesh(
        mesh.devices.reshape(n_chips // 2, 2, 2, mesh.shape["expert"]), ("zz", "h", "c", "expert")
    )
    dp = ("zz", "h", "c")
    placed = (
        P((*dp, "expert"), None),
        P(dp, "expert"),
        P(dp, None, "expert"),
        P(dp, None, "expert"),
        P(dp, None),
        P(dp, None),
        P(dp, None),
        P("expert", None),
        P(),
        P(),
        P("expert", dp, None),
        P("expert", dp, None),
        P("expert", dp, None),
        P((*dp, "expert"), None),
        P(),
    )

    return jax.shard_map(
        on_device,
        mesh=split,
        in_specs=placed,
        out_specs=(P((*dp, "expert"), None), P((*dp, "expert"), None)),
        check_vma=False,
    )
```
